32 devices in a mesh: seq: 8 (over z, x), head: 4 (over y, core).
Axes of the slice: x: 2, y: 2, z: 4, core: 2. Of those that a mesh axis runs over, the one named last changes fastest.
Arguments:
- query_act: bfloat16 [10240, 5120], P('seq', 'head'), may hold values from -5.5 to 5.5
- key_act: bfloat16 [10240, 5120], P('seq', 'head'), may hold values from -5.5 to 5.5
- value_act: bfloat16 [10240, 5120], P('seq', 'head'), may hold values from -6 to 6
- block_lists: int32 [80, 26], P('seq'), may hold values from -1 to 79, as said below
- key_stride: int32 [4], replicated, may hold values from 1 to 8, as said below
- out_weight: bfloat16 [5120, 5120], P('head'), may hold values from -0.3125 to 0.3125
Outputs:
- layer_out: bfloat16 [10240, 5120], P('seq', 'head')
The draws below stay inside these ranges and needn't reach their ends.
Inputs may be any that keep to these rules, and one draw needn't show every extreme that they name: `block_lists`: row i lists distinct key blocks: the 10 blocks of query block i's own frame and, for every frame at distance d of 1 to 3 on either side, max(1, 10 // 2**d) consecutive blocks of that frame; a slot holds -1 where that frame lies outside the clip. Slots stand in any order. `key_stride`: strides never fall as the distance grows; distance 0 has stride 1 and distance 3 has stride 8.
All inputs are finite; a program needn't handle non-finite values.
Results may differ from the reference program's by a relative error of at most 0.013.
Values may be sent and summed in bfloat16 or wider, within the bound.
No kernel may reach another device: no remote copies, remote signals or barrier semaphores. Data moves between devices by JAX's collectives and lax.ppermute only.
A program may use at most 192 MiB of HBM per device.

```python
import math
import jax
import jax.numpy as jnp
from jax import lax

D = 5120
HEADS = 40
HD = 128
BLK = 128
FRAME_BLK = 10
REACH = 3
NBLK = 80
TOKENS = 10240
FRAMES = 8
KMAX = 26
N_HEAD = 4


def drawn_rows(key, salt):
    return jnp.clip(1.4 * jax.random.normal(jax.random.fold_in(key, salt), (TOKENS, D)), -5.5, 5.5)


def draw_query_act(key, part):
    values_out = drawn_rows(key, 3)
    return values_out.astype(jnp.bfloat16)


def draw_key_act(key, part):
    values_out = drawn_rows(key, 4)
    return values_out.astype(jnp.bfloat16)


def draw_block_lists(key, part):
    blocks = jnp.arange(NBLK, dtype=jnp.int32)
    frame_of = blocks // FRAME_BLK
    place_in = blocks % FRAME_BLK
    columns = [frame_of[:, None] * FRAME_BLK + jnp.arange(FRAME_BLK, dtype=jnp.int32)[None, :]]
    counter = 0
    half_frame = FRAME_BLK // 2
    for direction in (-1, 1):
        for distance in range(1, REACH + 1):
            window_width = max(1, FRAME_BLK >> distance)
            counter = counter + 1
            jitter = jax.random.randint(jax.random.fold_in(key, counter), (NBLK,), -half_frame, half_frame + 1)
            first_block = jnp.clip(place_in - window_width // 2 + jitter, 0, FRAME_BLK - window_width)
            other_frame = frame_of + direction * distance
            inside = (other_frame >= 0) & (other_frame < FRAMES)
            chosen = other_frame[:, None] * FRAME_BLK + first_block[:, None] + jnp.arange(window_width, dtype=jnp.int32)[None, :]
            columns.append(jnp.where(inside[:, None], chosen, -1))
    listing = jnp.concatenate(columns, axis=1).astype(jnp.int32)
    ranking = jax.random.randint(jax.random.fold_in(key, 99), (NBLK, KMAX), 0, 1 << 20) * KMAX + jnp.arange(KMAX, dtype=jnp.int32)[None, :]
    ordering = jnp.argsort(ranking, axis=1)
    return jnp.take_along_axis(listing, ordering, axis=1).astype(jnp.int32)


def draw_key_stride(key, part):
    strides = jnp.sort(jax.random.randint(key, (REACH + 1,), 1, 9))
    strides = strides.at[0].set(1).at[REACH].set(8)
    return strides.astype(jnp.int32)


def shard_levels(stream_key, extent, split, least, top_value):
    gain, own = 1.0, jax.random.fold_in(stream_key, 6)
    for position, shards_of in split:
        heights = jnp.exp(jax.random.uniform(jax.random.fold_in(own, position), (shards_of,), jnp.float32, least / len(split), top_value / len(split)))
        gain = gain * jnp.repeat(heights, extent[position] // shards_of).reshape([-1 if axis == position else 1 for axis in range(len(extent))])
    return gain


def bell_draw(own_key, shape, width, bound, shards=(), held_as=jnp.bfloat16):
    result = jax.random.normal(own_key, shape, jnp.float32) * width
    if len(shards) > 0:
        result = shard_levels(own_key, shape, shards, -0.22, 0.18) * result
    return jnp.clip(result, min=-bound, max=bound).astype(held_as)


def setup_inputs(seed: int = 0) -> dict:
    streams_of = jax.random.split(jax.random.key(seed), 7)
    return {
        "query_act": draw_query_act(jax.random.fold_in(streams_of[6], 71), 0),
        "key_act": draw_key_act(jax.random.fold_in(streams_of[6], 71), 0),
        "value_act": bell_draw(streams_of[2], (TOKENS, D), 1.0, 6.0, ((0, 8), (1, 4))),
        "block_lists": draw_block_lists(jax.random.fold_in(streams_of[6], 71), 0),
        "key_stride": draw_key_stride(jax.random.fold_in(streams_of[6], 71), 0),
        "out_weight": bell_draw(streams_of[5], (D, D), (D // 16) ** -0.5, 0.3125, ((0, 4),)),
    }


def reference(query_act, key_act, value_act, block_lists, key_stride, out_weight):
    score_scale = 1.0 / math.sqrt(HD)
    query_blocks = query_act.reshape(NBLK, BLK, HEADS, HD)
    key_blocks = key_act.reshape(NBLK, BLK, HEADS, HD)
    value_blocks = value_act.reshape(NBLK, BLK, HEADS, HD)
    in_block = jnp.arange(BLK, dtype=jnp.int32)
    levels = jnp.arange(REACH + 1, dtype=jnp.int32)

    def attend(packet):
        block_no, listing = packet
        usable = listing >= 0
        safe_rows = jnp.where(usable, listing, 0).astype(jnp.int32)
        distance = jnp.abs(block_no // FRAME_BLK - listing // FRAME_BLK)
        step_of = lax.optimization_barrier(jnp.sum(jnp.where(distance[:, None] == levels[None, :], key_stride[None, :], 0), axis=1))
        step_of = jnp.where(usable, step_of, 1)
        keep_key = (usable[:, None] & (in_block[None, :] % step_of[:, None] == 0)).reshape(-1)
        keys_here = key_blocks[safe_rows].reshape(KMAX * BLK, HEADS, HD).astype(jnp.float32)
        values_here = value_blocks[safe_rows].reshape(KMAX * BLK, HEADS, HD).astype(jnp.float32)
        query_here = query_blocks[block_no].astype(jnp.float32)
        scores = jnp.einsum('qhd,khd->hqk', query_here, keys_here) * score_scale
        kept_mask = keep_key[None, None, :]
        scores = jnp.where(kept_mask, scores, -1e+30)
        row_max = lax.optimization_barrier(jnp.max(scores, axis=2, keepdims=True))
        exps_kept = jnp.where(kept_mask, jnp.exp(scores - row_max), 0.0)
        row_total = lax.optimization_barrier(jnp.sum(exps_kept, axis=2))
        weights = lax.optimization_barrier(exps_kept.astype(jnp.bfloat16)).astype(jnp.float32)
        combined = jnp.einsum('hqk,khd->qhd', weights, values_here)
        combined = combined / jnp.transpose(row_total)[:, :, None]
        return combined.astype(jnp.bfloat16)
    attended = lax.map(attend, (jnp.arange(NBLK, dtype=jnp.int32), block_lists))
    attended = attended.reshape(TOKENS, D)
    group_width = D // N_HEAD
    layer_out = jnp.zeros((TOKENS, D), jnp.float32)
    for group in range(N_HEAD):
        low_end = group * group_width
        group_term = jnp.dot(attended[:, low_end:low_end + group_width], out_weight[low_end:low_end + group_width, :], preferred_element_type=jnp.float32)
        layer_out = layer_out + lax.optimization_barrier(group_term.astype(jnp.bfloat16)).astype(jnp.float32)
    return layer_out.astype(jnp.bfloat16)
```

```python
import functools
import math

import jax
import jax.numpy as jnp
from jax import lax
from jax.experimental import pallas as pl
from jax.experimental.pallas import tpu as pltpu
from jax.sharding import PartitionSpec as P

HD = 128
BLK = 128
FRAME_BLK = 10
REACH = 3
FAR_STRIDE = 8


def from_behind(shard, axis, by):
    peers = lax.axis_size(axis)
    pairs = [(i, i + by) for i in range(peers) if 0 <= i + by < peers]
    return lax.ppermute(shard, axis, pairs)


def spread_far(compact, rows):
    width = compact.shape[-1]
    grown = jnp.pad(compact.reshape(rows // FAR_STRIDE, 1, width), ((0, 0), (0, FAR_STRIDE - 1), (0, 0)))
    return grown.reshape(rows, width)


def band_window(act, reach_dev):
    rows = act.shape[0]
    pieces = []
    for offset in range(reach_dev, 0, -1):
        if offset == REACH:
            far = from_behind(act[::FAR_STRIDE], "seq", offset)
            pieces.append(spread_far(far, rows))
        else:
            pieces.append(from_behind(act, "seq", offset))
    pieces.append(act)
    for offset in range(1, reach_dev + 1):
        if offset == REACH:
            far = from_behind(act[::FAR_STRIDE], "seq", -offset)
            pieces.append(spread_far(far, rows))
        else:
            pieces.append(from_behind(act, "seq", -offset))
    return jnp.concatenate(pieces, axis=0)


def attend_kernel(rows_ref, q_ref, k_ref, v_ref, keep_ref, o_ref, m_sc, l_sc, acc_sc, *, heads, nslot, scale):
    i = pl.program_id(0)
    s = pl.program_id(1)

    @pl.when(s == 0)
    def _():
        m_sc[...] = jnp.full(m_sc.shape, -jnp.inf, jnp.float32)
        l_sc[...] = jnp.zeros(l_sc.shape, jnp.float32)
        acc_sc[...] = jnp.zeros(acc_sc.shape, jnp.float32)

    @pl.when(rows_ref[1, i * nslot + s] > 0)
    def _():
        keep = keep_ref[0] > 0.0
        for h in range(heads):
            cols = pl.ds(h * HD, HD)
            qh = q_ref[:, cols]
            kh = k_ref[:, cols]
            sc = lax.dot_general(qh, kh, (((1,), (1,)), ((), ())), preferred_element_type=jnp.float32)
            sc = jnp.where(keep, sc * scale, -jnp.inf)
            m_prev = m_sc[h]
            m_new = jnp.maximum(m_prev, jnp.max(sc, axis=1, keepdims=True))
            alpha = jnp.exp(m_prev - m_new)
            p = jnp.exp(sc - m_new)
            l_sc[h] = alpha * l_sc[h] + jnp.sum(p, axis=1, keepdims=True)
            pv = jnp.dot(p.astype(jnp.bfloat16), v_ref[:, cols], preferred_element_type=jnp.float32)
            acc_sc[:, cols] = alpha * acc_sc[:, cols] + pv
            m_sc[h] = m_new

    @pl.when(s == nslot - 1)
    def _():
        for h in range(heads):
            cols = pl.ds(h * HD, HD)
            o_ref[:, cols] = (acc_sc[:, cols] / l_sc[h]).astype(o_ref.dtype)


def attend(query, kwin, vwin, rows, live, keep):
    nq = query.shape[0] // BLK
    nslot = rows.shape[1]
    width = query.shape[1]
    heads = width // HD
    table = jnp.stack([rows.reshape(-1), live.reshape(-1)]).astype(jnp.int32)
    kernel = functools.partial(attend_kernel, heads=heads, nslot=nslot, scale=1.0 / math.sqrt(HD))
    q_spec = pl.BlockSpec((BLK, width), lambda i, s, t: (i, 0))
    kv_spec = pl.BlockSpec((BLK, width), lambda i, s, t: (t[0, i * nslot + s], 0))
    keep_spec = pl.BlockSpec((1, 1, BLK), lambda i, s, t: (i * nslot + s, 0, 0))
    return pl.pallas_call(
        kernel,
        out_shape=jax.ShapeDtypeStruct(query.shape, jnp.bfloat16),
        grid_spec=pltpu.PrefetchScalarGridSpec(
            num_scalar_prefetch=1,
            grid=(nq, nslot),
            in_specs=[q_spec, kv_spec, kv_spec, keep_spec],
            out_specs=pl.BlockSpec((BLK, width), lambda i, s, t: (i, 0)),
            scratch_shapes=[
                pltpu.VMEM((heads, BLK, 1), jnp.float32),
                pltpu.VMEM((heads, BLK, 1), jnp.float32),
                pltpu.VMEM((BLK, width), jnp.float32),
            ],
        ),
        compiler_params=pltpu.CompilerParams(dimension_semantics=("arbitrary", "arbitrary")),
        cost_estimate=pl.CostEstimate(
            flops=4 * query.shape[0] * nslot * BLK * width,
            transcendentals=query.shape[0] * nslot * BLK * heads,
            bytes_accessed=2 * nq * nslot * BLK * width * 2 + 2 * query.size * 2,
        ),
    )(table, query, kwin, vwin, keep.reshape(-1, 1, BLK))


def halving_scatter(partial_f32, axis):
    n = lax.axis_size(axis)
    me = lax.axis_index(axis)
    bits = n.bit_length() - 1
    rows, total = partial_f32.shape
    group = total // n
    held = partial_f32.astype(jnp.bfloat16).astype(jnp.float32)
    held = held.reshape((rows,) + (2,) * bits + (group,))
    for b in range(bits):
        dim = held.ndim - 2
        mine = (me >> b) & 1
        keep = lax.dynamic_index_in_dim(held, mine, axis=dim, keepdims=False)
        send = lax.dynamic_index_in_dim(held, 1 - mine, axis=dim, keepdims=False)
        pairs = [(i, i ^ (1 << b)) for i in range(n)]
        got = lax.ppermute(send.astype(jnp.bfloat16), axis, pairs)
        held = keep + got.astype(jnp.float32)
    return held.reshape(rows, group).astype(jnp.bfloat16)


def shards(query_act, key_act, value_act, block_lists, key_stride, out_weight):
    rows_here = query_act.shape[0]
    blocks_here = rows_here // BLK
    assert blocks_here == FRAME_BLK
    reach_dev = REACH
    kwin = band_window(key_act, reach_dev)
    vwin = band_window(value_act, reach_dev)

    seq_index = lax.axis_index("seq")
    first_block = (seq_index - reach_dev) * blocks_here
    query_blocks = seq_index * blocks_here + jnp.arange(blocks_here, dtype=jnp.int32)
    listed = -jnp.sort(-block_lists, axis=1)
    usable = listed >= 0
    slot_rows = listed - first_block
    last_row = jnp.min(jnp.where(usable, slot_rows, 1 << 20), axis=1, keepdims=True)
    slot_rows = jnp.where(usable, slot_rows, last_row)
    distance = jnp.abs(query_blocks[:, None] // FRAME_BLK - listed // FRAME_BLK)
    levels = jnp.arange(REACH + 1, dtype=jnp.int32)
    step_of = jnp.sum(
        jnp.where(distance[:, :, None] == levels[None, None, :], key_stride[None, None, :], 0),
        axis=2,
    )
    step_of = jnp.where(usable, step_of, 1)
    in_block = jnp.arange(BLK, dtype=jnp.int32)
    keep_key = usable[:, :, None] & (in_block[None, None, :] % step_of[:, :, None] == 0)

    attended = attend(
        query_act, kwin, vwin, slot_rows, usable.astype(jnp.int32), keep_key.astype(jnp.float32)
    )
    partial_sum = jnp.dot(attended, out_weight, preferred_element_type=jnp.float32)
    return halving_scatter(partial_sum, "head")


def solution(mesh):
    placed = (
        P("seq", "head"),
        P("seq", "head"),
        P("seq", "head"),
        P("seq", None),
        P(),
        P("head", None),
    )
    return jax.shard_map(
        shards, mesh=mesh, in_specs=placed, out_specs=P("seq", "head"), check_vma=False
    )
```

```python
import functools
import math

import jax
import jax.numpy as jnp
from jax import lax
from jax.experimental import pallas as pl
from jax.experimental.pallas import tpu as pltpu
from jax.sharding import PartitionSpec as P

HD = 128
BLK = 128
FRAME_BLK = 10
REACH = 3
FAR_STRIDE = 8


def from_behind(shard, axis, by):
    peers = lax.axis_size(axis)
    pairs = [(i, i + by) for i in range(peers) if 0 <= i + by < peers]
    return lax.ppermute(shard, axis, pairs)


def spread_far(compact, rows):
    width = compact.shape[-1]
    grown = jnp.pad(compact.reshape(rows // FAR_STRIDE, 1, width), ((0, 0), (0, FAR_STRIDE - 1), (0, 0)))
    return grown.reshape(rows, width)


def band_window(key_act, value_act, reach_dev):
    assert reach_dev == REACH == 3
    rows = key_act.shape[0]
    both = jnp.concatenate([key_act, value_act], axis=0)
    with_far = jnp.concatenate([key_act, value_act, key_act[::FAR_STRIDE], value_act[::FAR_STRIDE]], axis=0)
    half = rows // FAR_STRIDE

    def spread(got):
        return jnp.concatenate([spread_far(got[:half], rows), spread_far(got[half:], rows)], axis=0)

    up2 = from_behind(with_far, "seq", 2)
    down2 = from_behind(with_far, "seq", -2)
    up1 = from_behind(both, "seq", 1)
    down1 = from_behind(both, "seq", -1)
    up3 = from_behind(up2[2 * rows:], "seq", 1)
    down3 = from_behind(down2[2 * rows:], "seq", -1)
    pieces = [spread(up3), up2[: 2 * rows], up1, both, down1, down2[: 2 * rows], spread(down3)]
    return jnp.concatenate(pieces, axis=0)


SIDES = [(sign, d) for d in range(1, REACH + 1) for sign in (1, -1)]


def run_blocks(d):
    return max(1, FRAME_BLK // 2 ** d)


def own_kernel(q_ref, k_ref, v_ref, acc_ref, m_ref, l_ref, *, heads, scale):
    for h in range(heads):
        cols = pl.ds(h * HD, HD)
        sc = lax.dot_general(q_ref[:, cols], k_ref[:, cols], (((1,), (1,)), ((), ())), preferred_element_type=jnp.float32)
        sc = sc * scale
        m = jnp.max(sc, axis=1, keepdims=True)
        p = jnp.exp(sc - m)
        m_ref[:, h:h + 1] = m
        l_ref[:, h:h + 1] = jnp.sum(p, axis=1, keepdims=True)
        acc_ref[:, cols] = jnp.dot(p.astype(jnp.bfloat16), v_ref[:, cols], preferred_element_type=jnp.float32)


def attend_own(query, key_act, value_act):
    rows, width = query.shape
    heads = width // HD
    kernel = functools.partial(own_kernel, heads=heads, scale=1.0 / math.sqrt(HD))
    row_spec = pl.BlockSpec((BLK, width), lambda i: (i, 0))
    frame_spec = pl.BlockSpec((rows, width), lambda i: (0, 0))
    stat_spec = pl.BlockSpec((BLK, heads), lambda i: (i, 0))
    return pl.pallas_call(
        kernel,
        out_shape=(
            jax.ShapeDtypeStruct((rows, width), jnp.float32),
            jax.ShapeDtypeStruct((rows, heads), jnp.float32),
            jax.ShapeDtypeStruct((rows, heads), jnp.float32),
        ),
        grid=(rows // BLK,),
        in_specs=[row_spec, frame_spec, frame_spec],
        out_specs=(row_spec, stat_spec, stat_spec),
        compiler_params=pltpu.CompilerParams(dimension_semantics=("arbitrary",)),
        cost_estimate=pl.CostEstimate(
            flops=4 * rows * rows * width,
            transcendentals=rows * rows * heads,
            bytes_accessed=3 * rows * width * 2 + rows * width * 4,
        ),
    )(query, key_act, value_act)


def attend_kernel(t_ref, q_ref, acc1_ref, m1_ref, l1_ref, *refs, heads, scale):
    side_refs = refs[: 2 * len(SIDES)]
    mask_ref, o_ref, s_sc = refs[2 * len(SIDES):]
    chunks = []
    moff = 0
    for j, (sign, d) in enumerate(SIDES):
        n = run_blocks(d) * BLK
        chunks.append((side_refs[2 * j], side_refs[2 * j + 1], moff, n))
        moff += n
    for h in range(heads):
        cols = pl.ds(h * HD, HD)
        qh = q_ref[:, cols]
        m1 = m1_ref[:, h:h + 1]
        m = m1
        for k, v, mo, n in chunks:
            sc = lax.dot_general(qh, k[:, cols], (((1,), (1,)), ((), ())), preferred_element_type=jnp.float32)
            sc = sc * scale
            keep = mask_ref[0, :, mo:mo + n] > 0.0
            sc = jnp.where(keep, sc, -jnp.inf)
            s_sc[:, mo:mo + n] = sc
            m = jnp.maximum(m, jnp.max(sc, axis=1, keepdims=True))
        alpha = jnp.exp(m1 - m)
        total = alpha * l1_ref[:, h:h + 1]
        acc = alpha * acc1_ref[:, cols]
        for k, v, mo, n in chunks:
            p = jnp.exp(s_sc[:, mo:mo + n] - m)
            total = total + jnp.sum(p, axis=1, keepdims=True)
            acc = acc + jnp.dot(p.astype(jnp.bfloat16), v[:, cols], preferred_element_type=jnp.float32)
        o_ref[:, cols] = (acc / total).astype(o_ref.dtype)


def attend(query, own, kvwin, starts, masks, rows_here):
    acc1, m1, l1 = own
    nq = query.shape[0] // BLK
    width = query.shape[1]
    heads = width // HD
    kernel = functools.partial(attend_kernel, heads=heads, scale=1.0 / math.sqrt(HD))
    q_spec = pl.BlockSpec((BLK, width), lambda i, t: (i, 0))
    stat_spec = pl.BlockSpec((BLK, heads), lambda i, t: (i, 0))
    side_specs = []
    side_args = []
    for j, (sign, d) in enumerate(SIDES):
        n = run_blocks(d) * BLK
        kspec = pl.BlockSpec((pl.Element(n), pl.Element(width)), lambda i, t, j=j: (pl.multiple_of(t[j, i], BLK), 0))
        vspec = pl.BlockSpec(
            (pl.Element(n), pl.Element(width)), lambda i, t, j=j: (pl.multiple_of(t[j, i] + rows_here, BLK), 0)
        )
        side_specs += [kspec, vspec]
        side_args += [kvwin, kvwin]
    nmask = masks.shape[-1]
    return pl.pallas_call(
        kernel,
        out_shape=jax.ShapeDtypeStruct(query.shape, jnp.bfloat16),
        grid_spec=pltpu.PrefetchScalarGridSpec(
            num_scalar_prefetch=1,
            grid=(nq,),
            in_specs=[q_spec, q_spec, stat_spec, stat_spec] + side_specs + [pl.BlockSpec((1, 1, nmask), lambda i, t: (i, 0, 0))],
            out_specs=pl.BlockSpec((BLK, width), lambda i, t: (i, 0)),
            scratch_shapes=[pltpu.VMEM((BLK, nmask), jnp.float32)],
        ),
        compiler_params=pltpu.CompilerParams(dimension_semantics=("arbitrary",)),
        cost_estimate=pl.CostEstimate(
            flops=4 * query.shape[0] * nmask * width,
            transcendentals=query.shape[0] * nmask * heads,
            bytes_accessed=2 * nq * nmask * width * 2 + query.size * 8,
        ),
    )(starts, query, acc1, m1, l1, *side_args, masks)


def halving_scatter(attended, out_weight, axis):
    n = lax.axis_size(axis)
    me = lax.axis_index(axis)
    bits = n.bit_length() - 1
    group = out_weight.shape[1] // n

    def term(o):
        cols = lax.dynamic_slice_in_dim(out_weight, o * group, group, axis=1)
        t = jnp.dot(attended, cols, preferred_element_type=jnp.float32)
        return lax.optimization_barrier(t.astype(jnp.bfloat16)).astype(jnp.float32)

    level = term
    for b in range(bits):
        mb = (me >> b) & 1
        payload = jnp.stack([level(2 * k + 1 - mb).astype(jnp.bfloat16) for k in range(n >> (b + 1))])
        pairs = [(i, i ^ (1 << b)) for i in range(n)]
        got = lax.ppermute(payload, axis, pairs)

        def level(k, below=level, mb=mb, got=got):
            return below(2 * k + mb) + lax.dynamic_index_in_dim(got, k, axis=0, keepdims=False).astype(jnp.float32)

    return level(0).astype(jnp.bfloat16)


def shards(query_act, key_act, value_act, block_lists, key_stride, out_weight):
    rows_here = query_act.shape[0]
    blocks_here = rows_here // BLK
    assert blocks_here == FRAME_BLK
    reach_dev = REACH
    kvwin = band_window(key_act, value_act, reach_dev)

    seq_index = lax.axis_index("seq")
    first_block = (seq_index - reach_dev) * blocks_here
    my_frame = seq_index * blocks_here // FRAME_BLK
    usable = block_lists >= 0
    rel = jnp.where(usable, block_lists // FRAME_BLK - my_frame, 0)
    in_block = jnp.arange(BLK, dtype=jnp.int32)
    starts = []
    masks = []
    for sign, d in SIDES:
        picked = usable & (rel == sign * d)
        present = jnp.any(picked, axis=1)
        first = jnp.min(jnp.where(picked, block_lists, 1 << 20), axis=1)
        place = first - first_block
        row = (place // blocks_here) * (2 * rows_here) + (place % blocks_here) * BLK
        starts.append(jnp.where(present, row, 0))
        kept = (in_block % key_stride[d]) == 0
        kept = jnp.tile(kept, run_blocks(d))
        masks.append(present[:, None] & kept[None, :])
    starts = jnp.stack(starts).astype(jnp.int32)
    masks = jnp.concatenate(masks, axis=1).astype(jnp.float32)
    masks = masks[:, None, :]
    own = attend_own(query_act, key_act, value_act)
    cut = blocks_here // 2
    outs = []
    for lo, hi in ((0, cut), (cut, blocks_here)):
        part = tuple(a[lo * BLK:hi * BLK] for a in own)
        attended = attend(query_act[lo * BLK:hi * BLK], part, kvwin, starts[:, lo:hi], masks[lo:hi], rows_here)
        outs.append(halving_scatter(attended, out_weight, "head"))
    return jnp.concatenate(outs, axis=0)


def solution(mesh):
    placed = (
        P("seq", "head"),
        P("seq", "head"),
        P("seq", "head"),
        P("seq", None),
        P(),
        P("head", None),
    )
    return jax.shard_map(
        shards, mesh=mesh, in_specs=placed, out_specs=P("seq", "head"), check_vma=False
    )
```

```python
import functools
import math

import jax
import jax.numpy as jnp
from jax import lax
from jax.experimental import pallas as pl
from jax.experimental.pallas import tpu as pltpu
from jax.sharding import PartitionSpec as P

HD = 128
BLK = 128
FRAME_BLK = 10
REACH = 3
FAR_STRIDE = 8


def from_behind(shard, axis, by):
    peers = lax.axis_size(axis)
    pairs = [(i, i + by) for i in range(peers) if 0 <= i + by < peers]
    return lax.ppermute(shard, axis, pairs)


def spread_far(compact, rows):
    width = compact.shape[-1]
    grown = jnp.pad(compact.reshape(rows // FAR_STRIDE, 1, width), ((0, 0), (0, FAR_STRIDE - 1), (0, 0)))
    return grown.reshape(rows, width)


def band_window(key_act, value_act, reach_dev):
    assert reach_dev == REACH == 3
    rows = key_act.shape[0]
    both = jnp.concatenate([key_act, value_act], axis=0)
    with_far = jnp.concatenate([key_act, value_act, key_act[::FAR_STRIDE], value_act[::FAR_STRIDE]], axis=0)
    half = rows // FAR_STRIDE

    def spread(got):
        return jnp.concatenate([spread_far(got[:half], rows), spread_far(got[half:], rows)], axis=0)

    up2 = from_behind(with_far, "seq", 2)
    down2 = from_behind(with_far, "seq", -2)
    up1 = from_behind(both, "seq", 1)
    down1 = from_behind(both, "seq", -1)
    up3 = from_behind(up2[2 * rows:], "seq", 1)
    down3 = from_behind(down2[2 * rows:], "seq", -1)
    pieces = [spread(up3), up2[: 2 * rows], up1, both, down1, down2[: 2 * rows], spread(down3)]
    return jnp.concatenate(pieces, axis=0)


SIDES = [(sign, d) for d in range(1, REACH + 1) for sign in (1, -1)]


def run_blocks(d):
    return max(1, FRAME_BLK // 2 ** d)


def own_kernel(q_ref, k_ref, v_ref, acc_ref, m_ref, l_ref, *, heads, scale):
    for h in range(heads):
        cols = pl.ds(h * HD, HD)
        sc = lax.dot_general(q_ref[:, cols], k_ref[:, cols], (((1,), (1,)), ((), ())), preferred_element_type=jnp.float32)
        sc = sc * scale
        m = jnp.max(sc, axis=1, keepdims=True)
        p = jnp.exp(sc - m)
        m_ref[:, h:h + 1] = m
        l_ref[:, h:h + 1] = jnp.sum(p, axis=1, keepdims=True)
        acc_ref[:, cols] = jnp.dot(p.astype(jnp.bfloat16), v_ref[:, cols], preferred_element_type=jnp.float32)


def attend_own(query, key_act, value_act):
    rows, width = query.shape
    heads = width // HD
    kernel = functools.partial(own_kernel, heads=heads, scale=1.0 / math.sqrt(HD))
    row_spec = pl.BlockSpec((BLK, width), lambda i: (i, 0))
    frame_spec = pl.BlockSpec((rows, width), lambda i: (0, 0))
    stat_spec = pl.BlockSpec((BLK, heads), lambda i: (i, 0))
    return pl.pallas_call(
        kernel,
        out_shape=(
            jax.ShapeDtypeStruct((rows, width), jnp.float32),
            jax.ShapeDtypeStruct((rows, heads), jnp.float32),
            jax.ShapeDtypeStruct((rows, heads), jnp.float32),
        ),
        grid=(rows // BLK,),
        in_specs=[row_spec, frame_spec, frame_spec],
        out_specs=(row_spec, stat_spec, stat_spec),
        compiler_params=pltpu.CompilerParams(dimension_semantics=("arbitrary",)),
        cost_estimate=pl.CostEstimate(
            flops=4 * rows * rows * width,
            transcendentals=rows * rows * heads,
            bytes_accessed=3 * rows * width * 2 + rows * width * 4,
        ),
    )(query, key_act, value_act)


def attend_kernel(t_ref, q_ref, acc1_ref, m1_ref, l1_ref, *refs, heads, scale):
    side_refs = refs[: 2 * len(SIDES)]
    mask_ref, o_ref, s_sc = refs[2 * len(SIDES):]
    chunks = []
    moff = 0
    for j, (sign, d) in enumerate(SIDES):
        n = run_blocks(d) * BLK
        chunks.append((side_refs[2 * j], side_refs[2 * j + 1], moff, n))
        moff += n
    lanes = lax.broadcasted_iota(jnp.int32, (BLK, heads), 1)

    def one_head(h, carry):
        cols = pl.ds(pl.multiple_of(h * HD, HD), HD)
        qh = q_ref[:, cols]
        pick = lanes == h
        m1 = jnp.sum(jnp.where(pick, m1_ref[...], 0.0), axis=1, keepdims=True)
        l1 = jnp.sum(jnp.where(pick, l1_ref[...], 0.0), axis=1, keepdims=True)
        m = m1
        for k, v, mo, n in chunks:
            sc = lax.dot_general(qh, k[:, cols], (((1,), (1,)), ((), ())), preferred_element_type=jnp.float32)
            sc = sc * scale
            keep = mask_ref[0, :, mo:mo + n] > 0.0
            sc = jnp.where(keep, sc, -jnp.inf)
            s_sc[:, mo:mo + n] = sc
            m = jnp.maximum(m, jnp.max(sc, axis=1, keepdims=True))
        alpha = jnp.exp(m1 - m)
        total = alpha * l1
        acc = alpha * acc1_ref[:, cols]
        for k, v, mo, n in chunks:
            p = jnp.exp(s_sc[:, mo:mo + n] - m)
            total = total + jnp.sum(p, axis=1, keepdims=True)
            acc = acc + jnp.dot(p.astype(jnp.bfloat16), v[:, cols], preferred_element_type=jnp.float32)
        o_ref[:, cols] = (acc / total).astype(o_ref.dtype)
        return carry

    lax.fori_loop(0, heads, one_head, 0)


def attend(query, own, kvwin, starts, masks, rows_here):
    acc1, m1, l1 = own
    nq = query.shape[0] // BLK
    width = query.shape[1]
    heads = width // HD
    kernel = functools.partial(attend_kernel, heads=heads, scale=1.0 / math.sqrt(HD))
    q_spec = pl.BlockSpec((BLK, width), lambda i, t: (i, 0))
    stat_spec = pl.BlockSpec((BLK, heads), lambda i, t: (i, 0))
    side_specs = []
    side_args = []
    for j, (sign, d) in enumerate(SIDES):
        n = run_blocks(d) * BLK
        kspec = pl.BlockSpec((pl.Element(n), pl.Element(width)), lambda i, t, j=j: (pl.multiple_of(t[j, i], BLK), 0))
        vspec = pl.BlockSpec(
            (pl.Element(n), pl.Element(width)), lambda i, t, j=j: (pl.multiple_of(t[j, i] + rows_here, BLK), 0)
        )
        side_specs += [kspec, vspec]
        side_args += [kvwin, kvwin]
    nmask = masks.shape[-1]
    return pl.pallas_call(
        kernel,
        out_shape=jax.ShapeDtypeStruct(query.shape, jnp.bfloat16),
        grid_spec=pltpu.PrefetchScalarGridSpec(
            num_scalar_prefetch=1,
            grid=(nq,),
            in_specs=[q_spec, q_spec, stat_spec, stat_spec] + side_specs + [pl.BlockSpec((1, 1, nmask), lambda i, t: (i, 0, 0))],
            out_specs=pl.BlockSpec((BLK, width), lambda i, t: (i, 0)),
            scratch_shapes=[pltpu.VMEM((BLK, nmask), jnp.float32)],
        ),
        compiler_params=pltpu.CompilerParams(dimension_semantics=("arbitrary",)),
        cost_estimate=pl.CostEstimate(
            flops=4 * query.shape[0] * nmask * width,
            transcendentals=query.shape[0] * nmask * heads,
            bytes_accessed=2 * nq * nmask * width * 2 + query.size * 8,
        ),
    )(starts, query, acc1, m1, l1, *side_args, masks)


def halving_scatter(attended, out_weight, axis):
    n = lax.axis_size(axis)
    me = lax.axis_index(axis)
    bits = n.bit_length() - 1
    group = out_weight.shape[1] // n

    def term(o):
        cols = lax.dynamic_slice_in_dim(out_weight, o * group, group, axis=1)
        t = jnp.dot(attended, cols, preferred_element_type=jnp.float32)
        return lax.optimization_barrier(t.astype(jnp.bfloat16)).astype(jnp.float32)

    level = term
    for b in range(bits):
        mb = (me >> b) & 1
        payload = jnp.stack([level(2 * k + 1 - mb).astype(jnp.bfloat16) for k in range(n >> (b + 1))])
        pairs = [(i, i ^ (1 << b)) for i in range(n)]
        got = lax.ppermute(payload, axis, pairs)

        def level(k, below=level, mb=mb, got=got):
            return below(2 * k + mb) + lax.dynamic_index_in_dim(got, k, axis=0, keepdims=False).astype(jnp.float32)

    return level(0).astype(jnp.bfloat16)


def shards(query_act, key_act, value_act, block_lists, key_stride, out_weight):
    rows_here = query_act.shape[0]
    blocks_here = rows_here // BLK
    assert blocks_here == FRAME_BLK
    reach_dev = REACH
    kvwin = band_window(key_act, value_act, reach_dev)

    seq_index = lax.axis_index("seq")
    first_block = (seq_index - reach_dev) * blocks_here
    my_frame = seq_index * blocks_here // FRAME_BLK
    usable = block_lists >= 0
    rel = jnp.where(usable, block_lists // FRAME_BLK - my_frame, 0)
    in_block = jnp.arange(BLK, dtype=jnp.int32)
    starts = []
    masks = []
    for sign, d in SIDES:
        picked = usable & (rel == sign * d)
        present = jnp.any(picked, axis=1)
        first = jnp.min(jnp.where(picked, block_lists, 1 << 20), axis=1)
        place = first - first_block
        row = (place // blocks_here) * (2 * rows_here) + (place % blocks_here) * BLK
        starts.append(jnp.where(present, row, 0))
        kept = (in_block % key_stride[d]) == 0
        kept = jnp.tile(kept, run_blocks(d))
        masks.append(present[:, None] & kept[None, :])
    starts = jnp.stack(starts).astype(jnp.int32)
    masks = jnp.concatenate(masks, axis=1).astype(jnp.float32)
    masks = masks[:, None, :]
    own = attend_own(query_act, key_act, value_act)
    cut = blocks_here // 2
    outs = []
    for lo, hi in ((0, cut), (cut, blocks_here)):
        part = tuple(a[lo * BLK:hi * BLK] for a in own)
        attended = attend(query_act[lo * BLK:hi * BLK], part, kvwin, starts[:, lo:hi], masks[lo:hi], rows_here)
        outs.append(halving_scatter(attended, out_weight, "head"))
    return jnp.concatenate(outs, axis=0)


def solution(mesh):
    placed = (
        P("seq", "head"),
        P("seq", "head"),
        P("seq", "head"),
        P("seq", None),
        P(),
        P("head", None),
    )
    return jax.shard_map(
        shards, mesh=mesh, in_specs=placed, out_specs=P("seq", "head"), check_vma=False
    )
```

```python
import functools
import math

import jax
import jax.numpy as jnp
from jax import lax
from jax.experimental import pallas as pl
from jax.experimental.pallas import tpu as pltpu
from jax.sharding import PartitionSpec as P

HD = 128
BLK = 128
FRAME_BLK = 10
REACH = 3
FAR_STRIDE = 8


def from_behind(shard, axis, by):
    peers = lax.axis_size(axis)
    pairs = [(i, i + by) for i in range(peers) if 0 <= i + by < peers]
    return lax.ppermute(shard, axis, pairs)


def spread_far(compact, rows):
    width = compact.shape[-1]
    grown = jnp.pad(compact.reshape(rows // FAR_STRIDE, 1, width), ((0, 0), (0, FAR_STRIDE - 1), (0, 0)))
    return grown.reshape(rows, width)


def band_window(key_act, value_act, reach_dev):
    assert reach_dev == REACH == 3
    rows = key_act.shape[0]
    both = jnp.concatenate([key_act, value_act], axis=0)
    with_far = jnp.concatenate([key_act, value_act, key_act[::FAR_STRIDE], value_act[::FAR_STRIDE]], axis=0)
    half = rows // FAR_STRIDE

    def spread(got):
        return jnp.concatenate([spread_far(got[:half], rows), spread_far(got[half:], rows)], axis=0)

    up2 = from_behind(with_far, "seq", 2)
    down2 = from_behind(with_far, "seq", -2)
    up1 = from_behind(both, "seq", 1)
    down1 = from_behind(both, "seq", -1)
    up3 = from_behind(up2[2 * rows:], "seq", 1)
    down3 = from_behind(down2[2 * rows:], "seq", -1)
    return {(1, 1): down1, (-1, 1): up1, (1, 2): down2, (-1, 2): up2, (1, 3): spread(down3), (-1, 3): spread(up3)}


SIDES = [(sign, d) for d in range(1, REACH + 1) for sign in (1, -1)]


def run_blocks(d):
    return max(1, FRAME_BLK // 2 ** d)


def own_kernel(q_ref, k_ref, v_ref, acc_ref, m_ref, l_ref, *, heads, scale):
    for h in range(heads):
        cols = pl.ds(h * HD, HD)
        sc = lax.dot_general(q_ref[:, cols], k_ref[:, cols], (((1,), (1,)), ((), ())), preferred_element_type=jnp.float32)
        sc = sc * scale
        m = jnp.max(sc, axis=1, keepdims=True)
        p = jnp.exp(sc - m)
        m_ref[:, h:h + 1] = m
        l_ref[:, h:h + 1] = jnp.sum(p, axis=1, keepdims=True)
        acc_ref[:, cols] = jnp.dot(p.astype(jnp.bfloat16), v_ref[:, cols], preferred_element_type=jnp.float32)


def attend_own(query, key_act, value_act):
    rows, width = query.shape
    heads = width // HD
    kernel = functools.partial(own_kernel, heads=heads, scale=1.0 / math.sqrt(HD))
    row_spec = pl.BlockSpec((BLK, width), lambda i: (i, 0))
    frame_spec = pl.BlockSpec((rows, width), lambda i: (0, 0))
    stat_spec = pl.BlockSpec((BLK, heads), lambda i: (i, 0))
    return pl.pallas_call(
        kernel,
        out_shape=(
            jax.ShapeDtypeStruct((rows, width), jnp.float32),
            jax.ShapeDtypeStruct((rows, heads), jnp.float32),
            jax.ShapeDtypeStruct((rows, heads), jnp.float32),
        ),
        grid=(rows // BLK,),
        in_specs=[row_spec, frame_spec, frame_spec],
        out_specs=(row_spec, stat_spec, stat_spec),
        compiler_params=pltpu.CompilerParams(dimension_semantics=("arbitrary",)),
        cost_estimate=pl.CostEstimate(
            flops=4 * rows * rows * width,
            transcendentals=rows * rows * heads,
            bytes_accessed=3 * rows * width * 2 + rows * width * 4,
        ),
    )(query, key_act, value_act)


def attend_kernel(t_ref, q_ref, acc1_ref, m1_ref, l1_ref, *refs, heads, scale):
    side_refs = refs[: 2 * len(SIDES)]
    mask_ref, o_ref, s_sc = refs[2 * len(SIDES):]
    chunks = []
    moff = 0
    for j, (sign, d) in enumerate(SIDES):
        n = run_blocks(d) * BLK
        chunks.append((side_refs[2 * j], side_refs[2 * j + 1], moff, n))
        moff += n
    for h in range(heads):
        cols = pl.ds(h * HD, HD)
        qh = q_ref[:, cols]
        m1 = m1_ref[:, h:h + 1]
        m = m1
        for k, v, mo, n in chunks:
            sc = lax.dot_general(qh, k[:, cols], (((1,), (1,)), ((), ())), preferred_element_type=jnp.float32)
            sc = sc * scale
            keep = mask_ref[0, :, mo:mo + n] > 0.0
            sc = jnp.where(keep, sc, -jnp.inf)
            s_sc[:, mo:mo + n] = sc
            m = jnp.maximum(m, jnp.max(sc, axis=1, keepdims=True))
        alpha = jnp.exp(m1 - m)
        total = alpha * l1_ref[:, h:h + 1]
        acc = alpha * acc1_ref[:, cols]
        for k, v, mo, n in chunks:
            p = jnp.exp(s_sc[:, mo:mo + n] - m)
            total = total + jnp.sum(p, axis=1, keepdims=True)
            acc = acc + jnp.dot(p.astype(jnp.bfloat16), v[:, cols], preferred_element_type=jnp.float32)
        o_ref[:, cols] = (acc / total).astype(o_ref.dtype)


def attend(query, own, sides, starts, masks, rows_here):
    acc1, m1, l1 = own
    nq = query.shape[0] // BLK
    width = query.shape[1]
    heads = width // HD
    kernel = functools.partial(attend_kernel, heads=heads, scale=1.0 / math.sqrt(HD))
    q_spec = pl.BlockSpec((BLK, width), lambda i, t: (i, 0))
    stat_spec = pl.BlockSpec((BLK, heads), lambda i, t: (i, 0))
    side_specs = []
    side_args = []
    for j, (sign, d) in enumerate(SIDES):
        n = run_blocks(d) * BLK
        kspec = pl.BlockSpec((pl.Element(n), pl.Element(width)), lambda i, t, j=j: (pl.multiple_of(t[j, i], BLK), 0))
        vspec = pl.BlockSpec(
            (pl.Element(n), pl.Element(width)), lambda i, t, j=j: (pl.multiple_of(t[j, i] + rows_here, BLK), 0)
        )
        side_specs += [kspec, vspec]
        side_args += [sides[(sign, d)], sides[(sign, d)]]
    nmask = masks.shape[-1]
    return pl.pallas_call(
        kernel,
        out_shape=jax.ShapeDtypeStruct(query.shape, jnp.bfloat16),
        grid_spec=pltpu.PrefetchScalarGridSpec(
            num_scalar_prefetch=1,
            grid=(nq,),
            in_specs=[q_spec, q_spec, stat_spec, stat_spec] + side_specs + [pl.BlockSpec((1, 1, nmask), lambda i, t: (i, 0, 0))],
            out_specs=pl.BlockSpec((BLK, width), lambda i, t: (i, 0)),
            scratch_shapes=[pltpu.VMEM((BLK, nmask), jnp.float32)],
        ),
        compiler_params=pltpu.CompilerParams(dimension_semantics=("arbitrary",)),
        cost_estimate=pl.CostEstimate(
            flops=4 * query.shape[0] * nmask * width,
            transcendentals=query.shape[0] * nmask * heads,
            bytes_accessed=2 * nq * nmask * width * 2 + query.size * 8,
        ),
    )(starts, query, acc1, m1, l1, *side_args, masks)


def halving_scatter(attended, out_weight, axis):
    n = lax.axis_size(axis)
    me = lax.axis_index(axis)
    bits = n.bit_length() - 1
    group = out_weight.shape[1] // n

    def term(o):
        cols = lax.dynamic_slice_in_dim(out_weight, o * group, group, axis=1)
        t = jnp.dot(attended, cols, preferred_element_type=jnp.float32)
        return lax.optimization_barrier(t.astype(jnp.bfloat16)).astype(jnp.float32)

    level = term
    for b in range(bits):
        mb = (me >> b) & 1
        payload = jnp.stack([level(2 * k + 1 - mb).astype(jnp.bfloat16) for k in range(n >> (b + 1))])
        pairs = [(i, i ^ (1 << b)) for i in range(n)]
        got = lax.ppermute(payload, axis, pairs)

        def level(k, below=level, mb=mb, got=got):
            return below(2 * k + mb) + lax.dynamic_index_in_dim(got, k, axis=0, keepdims=False).astype(jnp.float32)

    return level(0).astype(jnp.bfloat16)


def shards(query_act, key_act, value_act, block_lists, key_stride, out_weight):
    rows_here = query_act.shape[0]
    blocks_here = rows_here // BLK
    assert blocks_here == FRAME_BLK
    reach_dev = REACH
    sides = band_window(key_act, value_act, reach_dev)

    seq_index = lax.axis_index("seq")
    first_block = (seq_index - reach_dev) * blocks_here
    my_frame = seq_index * blocks_here // FRAME_BLK
    usable = block_lists >= 0
    rel = jnp.where(usable, block_lists // FRAME_BLK - my_frame, 0)
    in_block = jnp.arange(BLK, dtype=jnp.int32)
    starts = []
    masks = []
    for sign, d in SIDES:
        picked = usable & (rel == sign * d)
        present = jnp.any(picked, axis=1)
        first = jnp.min(jnp.where(picked, block_lists, 1 << 20), axis=1)
        starts.append(jnp.where(present, (first % blocks_here) * BLK, 0))
        kept = (in_block % key_stride[d]) == 0
        kept = jnp.tile(kept, run_blocks(d))
        masks.append(present[:, None] & kept[None, :])
    starts = jnp.stack(starts).astype(jnp.int32)
    masks = jnp.concatenate(masks, axis=1).astype(jnp.float32)
    masks = masks[:, None, :]
    own = attend_own(query_act, key_act, value_act)
    cut = blocks_here // 2
    outs = []
    for lo, hi in ((0, cut), (cut, blocks_here)):
        part = tuple(a[lo * BLK:hi * BLK] for a in own)
        attended = attend(query_act[lo * BLK:hi * BLK], part, sides, starts[:, lo:hi], masks[lo:hi], rows_here)
        outs.append(halving_scatter(attended, out_weight, "head"))
    return jnp.concatenate(outs, axis=0)


def solution(mesh):
    placed = (
        P("seq", "head"),
        P("seq", "head"),
        P("seq", "head"),
        P("seq", None),
        P(),
        P("head", None),
    )
    return jax.shard_map(
        shards, mesh=mesh, in_specs=placed, out_specs=P("seq", "head"), check_vma=False
    )
```

```python
import functools
import math

import jax
import jax.numpy as jnp
from jax import lax
from jax.experimental import pallas as pl
from jax.experimental.pallas import tpu as pltpu
from jax.sharding import PartitionSpec as P

HD = 128
BLK = 128
FRAME_BLK = 10
REACH = 3
FAR_STRIDE = 8


def from_behind(shard, axis, by):
    peers = lax.axis_size(axis)
    pairs = [(i, i + by) for i in range(peers) if 0 <= i + by < peers]
    return lax.ppermute(shard, axis, pairs)


def spread_far(compact, rows):
    width = compact.shape[-1]
    grown = jnp.pad(compact.reshape(rows // FAR_STRIDE, 1, width), ((0, 0), (0, FAR_STRIDE - 1), (0, 0)))
    return grown.reshape(rows, width)


def band_window(key_act, value_act, reach_dev):
    assert reach_dev == REACH == 3
    rows = key_act.shape[0]
    both = jnp.concatenate([key_act, value_act], axis=0)
    with_far = jnp.concatenate([key_act, value_act, key_act[::FAR_STRIDE], value_act[::FAR_STRIDE]], axis=0)
    half = rows // FAR_STRIDE

    def spread(got):
        return jnp.concatenate([spread_far(got[:half], rows), spread_far(got[half:], rows)], axis=0)

    up2 = from_behind(with_far, "seq", 2)
    down2 = from_behind(with_far, "seq", -2)
    up1 = from_behind(both, "seq", 1)
    down1 = from_behind(both, "seq", -1)
    up3 = from_behind(up2[2 * rows:], "seq", 1)
    down3 = from_behind(down2[2 * rows:], "seq", -1)
    return {(1, 1): down1, (-1, 1): up1, (1, 2): down2, (-1, 2): up2, (1, 3): down3, (-1, 3): up3}


SIDES = [(sign, d) for d in range(1, REACH + 1) for sign in (1, -1)]


def run_blocks(d):
    return max(1, FRAME_BLK // 2 ** d)


def side_geometry(d, rows_here):
    unit = BLK // FAR_STRIDE if d == REACH else BLK
    keys = run_blocks(d) * unit
    shift = rows_here // FAR_STRIDE if d == REACH else rows_here
    return unit, keys, shift, -(-keys // BLK) * BLK


def own_kernel(q_ref, k_ref, v_ref, acc_ref, m_ref, l_ref, *, heads, scale):
    for h in range(heads):
        cols = pl.ds(h * HD, HD)
        sc = lax.dot_general(q_ref[:, cols], k_ref[:, cols], (((1,), (1,)), ((), ())), preferred_element_type=jnp.float32)
        sc = sc * scale
        m = jnp.max(sc, axis=1, keepdims=True)
        p = jnp.exp(sc - m)
        m_ref[:, h:h + 1] = m
        l_ref[:, h:h + 1] = jnp.sum(p, axis=1, keepdims=True)
        acc_ref[:, cols] = jnp.dot(p.astype(jnp.bfloat16), v_ref[:, cols], preferred_element_type=jnp.float32)


def attend_own(query, key_act, value_act):
    rows, width = query.shape
    heads = width // HD
    kernel = functools.partial(own_kernel, heads=heads, scale=1.0 / math.sqrt(HD))
    row_spec = pl.BlockSpec((BLK, width), lambda i: (i, 0))
    frame_spec = pl.BlockSpec((rows, width), lambda i: (0, 0))
    stat_spec = pl.BlockSpec((BLK, heads), lambda i: (i, 0))
    return pl.pallas_call(
        kernel,
        out_shape=(
            jax.ShapeDtypeStruct((rows, width), jnp.float32),
            jax.ShapeDtypeStruct((rows, heads), jnp.float32),
            jax.ShapeDtypeStruct((rows, heads), jnp.float32),
        ),
        grid=(rows // BLK,),
        in_specs=[row_spec, frame_spec, frame_spec],
        out_specs=(row_spec, stat_spec, stat_spec),
        compiler_params=pltpu.CompilerParams(dimension_semantics=("arbitrary",)),
        cost_estimate=pl.CostEstimate(
            flops=4 * rows * rows * width,
            transcendentals=rows * rows * heads,
            bytes_accessed=3 * rows * width * 2 + rows * width * 4,
        ),
    )(query, key_act, value_act)


def attend_kernel(t_ref, q_ref, acc1_ref, m1_ref, l1_ref, *refs, heads, scale, rows_here):
    side_refs = refs[: 2 * len(SIDES)]
    mask_ref, o_ref, s_sc = refs[2 * len(SIDES):]
    chunks = []
    moff = 0
    for j, (sign, d) in enumerate(SIDES):
        _, n, _, slot = side_geometry(d, rows_here)
        chunks.append((side_refs[2 * j], side_refs[2 * j + 1], moff, n))
        moff += slot
    for h in range(heads):
        cols = pl.ds(h * HD, HD)
        qh = q_ref[:, cols]
        m1 = m1_ref[:, h:h + 1]
        m = m1
        for k, v, mo, n in chunks:
            sc = lax.dot_general(qh, k[:, cols], (((1,), (1,)), ((), ())), preferred_element_type=jnp.float32)
            sc = sc * scale
            keep = mask_ref[0, :, mo:mo + n] > 0.0
            sc = jnp.where(keep, sc, -jnp.inf)
            s_sc[:, mo:mo + n] = sc
            m = jnp.maximum(m, jnp.max(sc, axis=1, keepdims=True))
        alpha = jnp.exp(m1 - m)
        total = alpha * l1_ref[:, h:h + 1]
        acc = alpha * acc1_ref[:, cols]
        for k, v, mo, n in chunks:
            p = jnp.exp(s_sc[:, mo:mo + n] - m)
            total = total + jnp.sum(p, axis=1, keepdims=True)
            acc = acc + jnp.dot(p.astype(jnp.bfloat16), v[:, cols], preferred_element_type=jnp.float32)
        o_ref[:, cols] = (acc / total).astype(o_ref.dtype)


def attend(query, own, sides, starts, masks, rows_here):
    acc1, m1, l1 = own
    nq = query.shape[0] // BLK
    width = query.shape[1]
    heads = width // HD
    kernel = functools.partial(attend_kernel, heads=heads, scale=1.0 / math.sqrt(HD), rows_here=rows_here)
    q_spec = pl.BlockSpec((BLK, width), lambda i, t: (i, 0))
    stat_spec = pl.BlockSpec((BLK, heads), lambda i, t: (i, 0))
    side_specs = []
    side_args = []
    for j, (sign, d) in enumerate(SIDES):
        unit, n, shift, _ = side_geometry(d, rows_here)
        kspec = pl.BlockSpec(
            (pl.Element(n), pl.Element(width)), lambda i, t, j=j, u=unit: (pl.multiple_of(t[j, i], u), 0)
        )
        vspec = pl.BlockSpec(
            (pl.Element(n), pl.Element(width)), lambda i, t, j=j, u=unit, s=shift: (pl.multiple_of(t[j, i] + s, u), 0)
        )
        side_specs += [kspec, vspec]
        side_args += [sides[(sign, d)], sides[(sign, d)]]
    nmask = masks.shape[-1]
    return pl.pallas_call(
        kernel,
        out_shape=jax.ShapeDtypeStruct(query.shape, jnp.bfloat16),
        grid_spec=pltpu.PrefetchScalarGridSpec(
            num_scalar_prefetch=1,
            grid=(nq,),
            in_specs=[q_spec, q_spec, stat_spec, stat_spec] + side_specs + [pl.BlockSpec((1, 1, nmask), lambda i, t: (i, 0, 0))],
            out_specs=pl.BlockSpec((BLK, width), lambda i, t: (i, 0)),
            scratch_shapes=[pltpu.VMEM((BLK, nmask), jnp.float32)],
        ),
        compiler_params=pltpu.CompilerParams(dimension_semantics=("arbitrary",)),
        cost_estimate=pl.CostEstimate(
            flops=4 * query.shape[0] * nmask * width,
            transcendentals=query.shape[0] * nmask * heads,
            bytes_accessed=2 * nq * nmask * width * 2 + query.size * 8,
        ),
    )(starts, query, acc1, m1, l1, *side_args, masks)


def halving_scatter(attended, out_weight, axis):
    n = lax.axis_size(axis)
    me = lax.axis_index(axis)
    bits = n.bit_length() - 1
    group = out_weight.shape[1] // n

    def term(o):
        cols = lax.dynamic_slice_in_dim(out_weight, o * group, group, axis=1)
        t = jnp.dot(attended, cols, preferred_element_type=jnp.float32)
        return lax.optimization_barrier(t.astype(jnp.bfloat16)).astype(jnp.float32)

    level = term
    for b in range(bits):
        mb = (me >> b) & 1
        payload = jnp.stack([level(2 * k + 1 - mb).astype(jnp.bfloat16) for k in range(n >> (b + 1))])
        pairs = [(i, i ^ (1 << b)) for i in range(n)]
        got = lax.ppermute(payload, axis, pairs)

        def level(k, below=level, mb=mb, got=got):
            return below(2 * k + mb) + lax.dynamic_index_in_dim(got, k, axis=0, keepdims=False).astype(jnp.float32)

    return level(0).astype(jnp.bfloat16)


def shards(query_act, key_act, value_act, block_lists, key_stride, out_weight):
    rows_here = query_act.shape[0]
    blocks_here = rows_here // BLK
    assert blocks_here == FRAME_BLK
    reach_dev = REACH
    sides = band_window(key_act, value_act, reach_dev)

    seq_index = lax.axis_index("seq")
    first_block = (seq_index - reach_dev) * blocks_here
    my_frame = seq_index * blocks_here // FRAME_BLK
    usable = block_lists >= 0
    rel = jnp.where(usable, block_lists // FRAME_BLK - my_frame, 0)
    in_block = jnp.arange(BLK, dtype=jnp.int32)
    starts = []
    masks = []
    for sign, d in SIDES:
        picked = usable & (rel == sign * d)
        present = jnp.any(picked, axis=1)
        first = jnp.min(jnp.where(picked, block_lists, 1 << 20), axis=1)
        unit, n, _, slot = side_geometry(d, rows_here)
        starts.append(jnp.where(present, (first % blocks_here) * unit, 0))
        if d == REACH:
            kept = jnp.arange(slot) < n
        else:
            kept = jnp.tile((in_block % key_stride[d]) == 0, run_blocks(d))
        masks.append(present[:, None] & kept[None, :])
    starts = jnp.stack(starts).astype(jnp.int32)
    masks = jnp.concatenate(masks, axis=1).astype(jnp.float32)
    masks = masks[:, None, :]
    own = attend_own(query_act, key_act, value_act)
    cut = blocks_here // 2
    outs = []
    for lo, hi in ((0, cut), (cut, blocks_here)):
        part = tuple(a[lo * BLK:hi * BLK] for a in own)
        attended = attend(query_act[lo * BLK:hi * BLK], part, sides, starts[:, lo:hi], masks[lo:hi], rows_here)
        outs.append(halving_scatter(attended, out_weight, "head"))
    return jnp.concatenate(outs, axis=0)


def solution(mesh):
    placed = (
        P("seq", "head"),
        P("seq", "head"),
        P("seq", "head"),
        P("seq", None),
        P(),
        P("head", None),
    )
    return jax.shard_map(
        shards, mesh=mesh, in_specs=placed, out_specs=P("seq", "head"), check_vma=False
    )
```

```python
import functools
import math

import jax
import jax.numpy as jnp
from jax import lax
from jax.experimental import pallas as pl
from jax.experimental.pallas import tpu as pltpu
from jax.sharding import PartitionSpec as P

HD = 128
BLK = 128
FRAME_BLK = 10
REACH = 3
FAR_STRIDE = 8


def from_behind(shard, axis, by):
    peers = lax.axis_size(axis)
    pairs = [(i, i + by) for i in range(peers) if 0 <= i + by < peers]
    return lax.ppermute(shard, axis, pairs)


def spread_far(compact, rows):
    width = compact.shape[-1]
    grown = jnp.pad(compact.reshape(rows // FAR_STRIDE, 1, width), ((0, 0), (0, FAR_STRIDE - 1), (0, 0)))
    return grown.reshape(rows, width)


def band_window(key_act, value_act, reach_dev):
    assert reach_dev == REACH == 3
    rows = key_act.shape[0]
    both = jnp.concatenate([key_act, value_act], axis=0)
    with_far = jnp.concatenate([key_act, value_act, key_act[::FAR_STRIDE], value_act[::FAR_STRIDE]], axis=0)
    half = rows // FAR_STRIDE

    def spread(got):
        return jnp.concatenate([spread_far(got[:half], rows), spread_far(got[half:], rows)], axis=0)

    up2 = from_behind(with_far, "seq", 2)
    down2 = from_behind(with_far, "seq", -2)
    up1 = from_behind(both, "seq", 1)
    down1 = from_behind(both, "seq", -1)
    up3 = from_behind(up2[2 * rows:], "seq", 1)
    down3 = from_behind(down2[2 * rows:], "seq", -1)
    return {(1, 1): down1, (-1, 1): up1, (1, 2): down2, (-1, 2): up2, (1, 3): down3, (-1, 3): up3}


SIDES = [(sign, d) for d in range(1, REACH + 1) for sign in (1, -1)]


def run_blocks(d):
    return max(1, FRAME_BLK // 2 ** d)


def side_geometry(d, rows_here):
    unit = BLK // FAR_STRIDE if d == REACH else BLK
    keys = run_blocks(d) * unit
    shift = rows_here // FAR_STRIDE if d == REACH else rows_here
    return unit, keys, shift, -(-keys // BLK) * BLK


def own_kernel(q_ref, k_ref, v_ref, acc_ref, m_ref, l_ref, *, heads, scale):
    lanes = lax.broadcasted_iota(jnp.int32, (BLK, heads), 1)

    def one_head(h, carry):
        m_all, l_all = carry
        cols = pl.ds(pl.multiple_of(h * HD, HD), HD)
        sc = lax.dot_general(q_ref[:, cols], k_ref[:, cols], (((1,), (1,)), ((), ())), preferred_element_type=jnp.float32)
        sc = sc * scale
        m = jnp.max(sc, axis=1, keepdims=True)
        p = jnp.exp(sc - m)
        acc_ref[:, cols] = jnp.dot(p.astype(jnp.bfloat16), v_ref[:, cols], preferred_element_type=jnp.float32)
        pick = lanes == h
        return jnp.where(pick, m, m_all), jnp.where(pick, jnp.sum(p, axis=1, keepdims=True), l_all)

    zero = jnp.zeros((BLK, heads), jnp.float32)
    m_all, l_all = lax.fori_loop(0, heads, one_head, (zero, zero))
    m_ref[...] = m_all
    l_ref[...] = l_all


def attend_own(query, key_act, value_act):
    rows, width = query.shape
    heads = width // HD
    kernel = functools.partial(own_kernel, heads=heads, scale=1.0 / math.sqrt(HD))
    row_spec = pl.BlockSpec((BLK, width), lambda i: (i, 0))
    frame_spec = pl.BlockSpec((rows, width), lambda i: (0, 0))
    stat_spec = pl.BlockSpec((BLK, heads), lambda i: (i, 0))
    return pl.pallas_call(
        kernel,
        out_shape=(
            jax.ShapeDtypeStruct((rows, width), jnp.float32),
            jax.ShapeDtypeStruct((rows, heads), jnp.float32),
            jax.ShapeDtypeStruct((rows, heads), jnp.float32),
        ),
        grid=(rows // BLK,),
        in_specs=[row_spec, frame_spec, frame_spec],
        out_specs=(row_spec, stat_spec, stat_spec),
        compiler_params=pltpu.CompilerParams(dimension_semantics=("arbitrary",)),
        cost_estimate=pl.CostEstimate(
            flops=4 * rows * rows * width,
            transcendentals=rows * rows * heads,
            bytes_accessed=3 * rows * width * 2 + rows * width * 4,
        ),
    )(query, key_act, value_act)


def attend_kernel(t_ref, q_ref, acc1_ref, m1_ref, l1_ref, *refs, heads, scale, rows_here):
    side_refs = refs[: 2 * len(SIDES)]
    mask_ref, o_ref, s_sc = refs[2 * len(SIDES):]
    chunks = []
    moff = 0
    for j, (sign, d) in enumerate(SIDES):
        _, n, _, slot = side_geometry(d, rows_here)
        chunks.append((side_refs[2 * j], side_refs[2 * j + 1], moff, n))
        moff += slot
    for h in range(heads):
        cols = pl.ds(h * HD, HD)
        qh = q_ref[:, cols]
        m1 = m1_ref[:, h:h + 1]
        m = m1
        for k, v, mo, n in chunks:
            sc = lax.dot_general(qh, k[:, cols], (((1,), (1,)), ((), ())), preferred_element_type=jnp.float32)
            sc = sc * scale
            keep = mask_ref[0, :, mo:mo + n] > 0.0
            sc = jnp.where(keep, sc, -jnp.inf)
            s_sc[:, mo:mo + n] = sc
            m = jnp.maximum(m, jnp.max(sc, axis=1, keepdims=True))
        alpha = jnp.exp(m1 - m)
        total = alpha * l1_ref[:, h:h + 1]
        acc = alpha * acc1_ref[:, cols]
        for k, v, mo, n in chunks:
            p = jnp.exp(s_sc[:, mo:mo + n] - m)
            total = total + jnp.sum(p, axis=1, keepdims=True)
            acc = acc + jnp.dot(p.astype(jnp.bfloat16), v[:, cols], preferred_element_type=jnp.float32)
        o_ref[:, cols] = (acc / total).astype(o_ref.dtype)


def attend(query, own, sides, starts, masks, rows_here):
    acc1, m1, l1 = own
    nq = query.shape[0] // BLK
    width = query.shape[1]
    heads = width // HD
    kernel = functools.partial(attend_kernel, heads=heads, scale=1.0 / math.sqrt(HD), rows_here=rows_here)
    q_spec = pl.BlockSpec((BLK, width), lambda i, t: (i, 0))
    stat_spec = pl.BlockSpec((BLK, heads), lambda i, t: (i, 0))
    side_specs = []
    side_args = []
    for j, (sign, d) in enumerate(SIDES):
        unit, n, shift, _ = side_geometry(d, rows_here)
        kspec = pl.BlockSpec(
            (pl.Element(n), pl.Element(width)), lambda i, t, j=j, u=unit: (pl.multiple_of(t[j, i], u), 0)
        )
        vspec = pl.BlockSpec(
            (pl.Element(n), pl.Element(width)), lambda i, t, j=j, u=unit, s=shift: (pl.multiple_of(t[j, i] + s, u), 0)
        )
        side_specs += [kspec, vspec]
        side_args += [sides[(sign, d)], sides[(sign, d)]]
    nmask = masks.shape[-1]
    return pl.pallas_call(
        kernel,
        out_shape=jax.ShapeDtypeStruct(query.shape, jnp.bfloat16),
        grid_spec=pltpu.PrefetchScalarGridSpec(
            num_scalar_prefetch=1,
            grid=(nq,),
            in_specs=[q_spec, q_spec, stat_spec, stat_spec] + side_specs + [pl.BlockSpec((1, 1, nmask), lambda i, t: (i, 0, 0))],
            out_specs=pl.BlockSpec((BLK, width), lambda i, t: (i, 0)),
            scratch_shapes=[pltpu.VMEM((BLK, nmask), jnp.float32)],
        ),
        compiler_params=pltpu.CompilerParams(dimension_semantics=("arbitrary",)),
        cost_estimate=pl.CostEstimate(
            flops=4 * query.shape[0] * nmask * width,
            transcendentals=query.shape[0] * nmask * heads,
            bytes_accessed=2 * nq * nmask * width * 2 + query.size * 8,
        ),
    )(starts, query, acc1, m1, l1, *side_args, masks)


def halving_scatter(attended, out_weight, axis):
    n = lax.axis_size(axis)
    me = lax.axis_index(axis)
    bits = n.bit_length() - 1
    group = out_weight.shape[1] // n

    def term(o):
        cols = lax.dynamic_slice_in_dim(out_weight, o * group, group, axis=1)
        t = jnp.dot(attended, cols, preferred_element_type=jnp.float32)
        return lax.optimization_barrier(t.astype(jnp.bfloat16)).astype(jnp.float32)

    level = term
    for b in range(bits):
        mb = (me >> b) & 1
        payload = jnp.stack([level(2 * k + 1 - mb).astype(jnp.bfloat16) for k in range(n >> (b + 1))])
        pairs = [(i, i ^ (1 << b)) for i in range(n)]
        got = lax.ppermute(payload, axis, pairs)

        def level(k, below=level, mb=mb, got=got):
            return below(2 * k + mb) + lax.dynamic_index_in_dim(got, k, axis=0, keepdims=False).astype(jnp.float32)

    return level(0).astype(jnp.bfloat16)


def shards(query_act, key_act, value_act, block_lists, key_stride, out_weight):
    rows_here = query_act.shape[0]
    blocks_here = rows_here // BLK
    assert blocks_here == FRAME_BLK
    reach_dev = REACH
    sides = band_window(key_act, value_act, reach_dev)

    seq_index = lax.axis_index("seq")
    first_block = (seq_index - reach_dev) * blocks_here
    my_frame = seq_index * blocks_here // FRAME_BLK
    usable = block_lists >= 0
    rel = jnp.where(usable, block_lists // FRAME_BLK - my_frame, 0)
    in_block = jnp.arange(BLK, dtype=jnp.int32)
    starts = []
    masks = []
    for sign, d in SIDES:
        picked = usable & (rel == sign * d)
        present = jnp.any(picked, axis=1)
        first = jnp.min(jnp.where(picked, block_lists, 1 << 20), axis=1)
        unit, n, _, slot = side_geometry(d, rows_here)
        starts.append(jnp.where(present, (first % blocks_here) * unit, 0))
        if d == REACH:
            kept = jnp.arange(slot) < n
        else:
            kept = jnp.tile((in_block % key_stride[d]) == 0, run_blocks(d))
        masks.append(present[:, None] & kept[None, :])
    starts = jnp.stack(starts).astype(jnp.int32)
    masks = jnp.concatenate(masks, axis=1).astype(jnp.float32)
    masks = masks[:, None, :]
    own = attend_own(query_act, key_act, value_act)
    cut = blocks_here // 2
    outs = []
    for lo, hi in ((0, cut), (cut, blocks_here)):
        part = tuple(a[lo * BLK:hi * BLK] for a in own)
        attended = attend(query_act[lo * BLK:hi * BLK], part, sides, starts[:, lo:hi], masks[lo:hi], rows_here)
        outs.append(halving_scatter(attended, out_weight, "head"))
    return jnp.concatenate(outs, axis=0)


def solution(mesh):
    placed = (
        P("seq", "head"),
        P("seq", "head"),
        P("seq", "head"),
        P("seq", None),
        P(),
        P("head", None),
    )
    return jax.shard_map(
        shards, mesh=mesh, in_specs=placed, out_specs=P("seq", "head"), check_vma=False
    )
```
